256 devices in a mesh: ta: 4 (over y), gz: 8 (over x, core), xy: 8 (over z).
Axes of the slice: x: 4, y: 4, z: 8, core: 2. Of those that a mesh axis runs over, the one named last changes fastest.
Arguments:
- right_side: bfloat16 [8, 16, 16, 2, 16, 128], P('ta', 'gz', 'xy'), may hold values from -40 to 40
- links: bfloat16 [8, 16, 16, 2, 9, 64, 128], P('ta', 'gz', 'xy'), may hold values from -4 to 8, as said below
Outputs:
- solution: float32 [8, 16, 16, 2, 16, 128], P('ta', 'gz', 'xy')
The draws below stay inside these ranges and needn't reach their ends.
Inputs may be any that keep to these rules, and one draw needn't show every extreme that they name: `links`: block entries; block 0 acts on the site itself.
All inputs are finite; a program needn't handle non-finite values.
Results may differ from the reference program's by a relative error of at most 0.008.
Values may be sent and summed in bfloat16 or wider, within the bound.
No kernel may reach another device: no remote copies, remote signals or barrier semaphores. Data moves between devices by JAX's collectives and lax.ppermute only.
A program may use at most 64 MiB of HBM per device.

```python
import math
import jax
import jax.numpy as jnp
from jax import lax

NC = 64
NRHS = 16
ITERS = 3
NT = 8
NZ = 16
NY = 16
NX = 2


def draw_links(key, part):
    key_noise, key_diag, key_level, key_tilt, key_overall = jax.random.split(key, 5)
    shape = (NT, NZ, NY, NX, 9, NC, 2 * NC)
    site_shape = (NT, NZ, NY, NX, 1, 1, 1)
    noise = jnp.clip(jax.random.normal(key_noise, shape, jnp.float32), -4.0, 4.0)
    level_low = 0.4
    level_high = 1.6
    block_index = jnp.arange(9, dtype=jnp.int32).reshape(9, 1, 1)
    row_index = jnp.arange(NC, dtype=jnp.int32).reshape(1, NC, 1)
    col_index = jnp.arange(2 * NC, dtype=jnp.int32).reshape(1, 1, 2 * NC)
    spread = jnp.where(block_index == 0, 0.02, 0.012)
    on_real = jnp.logical_and(block_index == 0, row_index == col_index)
    on_imag = jnp.logical_and(block_index == 0, row_index + NC == col_index)
    level_bit = jax.random.randint(key_level, site_shape, 0, 2).astype(jnp.float32)
    level = level_low + (level_high - level_low) * level_bit
    jitter = jnp.exp(jax.random.uniform(key_diag, site_shape, jnp.float32, math.log(0.85), math.log(1.18)))
    tilt = jax.random.uniform(key_tilt, site_shape, jnp.float32, -0.5, 0.5)
    diag_real = level * jitter
    diag_imag = diag_real * tilt
    t_pos = jnp.arange(NT, dtype=jnp.float32).reshape(NT, 1, 1, 1, 1, 1, 1) / NT
    z_pos = jnp.arange(NZ, dtype=jnp.float32).reshape(1, NZ, 1, 1, 1, 1, 1) / NZ
    y_pos = jnp.arange(NY, dtype=jnp.float32).reshape(1, 1, NY, 1, 1, 1, 1) / NY
    strength = 0.6 * jnp.exp(math.log(3.0) * (t_pos + z_pos + y_pos) / 3.0)
    overall = jnp.exp(jax.random.uniform(key_overall, (), jnp.float32, math.log(0.7), math.log(1.4)))
    base = spread * noise + jnp.where(on_real, diag_real, 0.0) + jnp.where(on_imag, diag_imag, 0.0)
    return (overall * strength * base).astype(jnp.bfloat16)


def draw_right_side(key, part):
    key_own, key_site, key_comp = jax.random.split(key, 3)
    shape = (NT, NZ, NY, NX, NRHS, 2 * NC)
    t_pos = jnp.arange(NT, dtype=jnp.float32).reshape(NT, 1, 1, 1, 1, 1) / NT
    z_pos = jnp.arange(NZ, dtype=jnp.float32).reshape(1, NZ, 1, 1, 1, 1) / NZ
    y_pos = jnp.arange(NY, dtype=jnp.float32).reshape(1, 1, NY, 1, 1, 1) / NY
    profile = 0.35 * jnp.exp(0.5 * math.log(3.0) * (t_pos + z_pos + y_pos))
    site_scale = jnp.exp(jax.random.uniform(key_site, (NT, NZ, NY, NX, 1, 1), jnp.float32, math.log(0.3), math.log(3.0)))
    comp_scale = jnp.exp(jax.random.uniform(key_comp, (1, 1, 1, 1, 1, 2 * NC), jnp.float32, math.log(0.5), math.log(2.0)))
    noise = jnp.clip(jax.random.normal(key_own, shape, jnp.float32), -4.0, 4.0)
    return (profile * site_scale * comp_scale * noise).astype(jnp.bfloat16)


def setup_inputs(seed: int = 0) -> dict:
    splits = jax.random.split(jax.random.key(seed), 3)
    right_side = draw_right_side(jax.random.fold_in(splits[2], 71), 0)
    links = draw_links(jax.random.fold_in(splits[2], 71), 0)
    return dict(right_side=right_side, links=links)


EPSILON = 1e-06

def turned(field):
    half = field.shape[-1] // 2
    return jnp.concatenate([-field[..., half:], field[..., :half]], axis=-1)

def inner_pair(left, right):
    return (lax.optimization_barrier(jnp.sum(left * right, axis=(0, 1, 2, 3, 5))), lax.optimization_barrier(jnp.sum(turned(left) * right, axis=(0, 1, 2, 3, 5))))

def combined(coef_re, coef_im, field):
    return coef_re[:, None] * field + coef_im[:, None] * turned(field)

def apply_operator(field, links):
    count_t = field.shape[0]
    half = field.shape[-1] // 2

    def one_slice(t_index):
        here = lax.dynamic_index_in_dim(field, t_index, 0, keepdims=False)
        ahead = lax.dynamic_index_in_dim(field, (t_index + 1) % count_t, 0, keepdims=False)
        behind = lax.dynamic_index_in_dim(field, (t_index + count_t - 1) % count_t, 0, keepdims=False)
        blocks = lax.dynamic_index_in_dim(links, t_index, 0, keepdims=False).astype(jnp.float32)
        near = jnp.stack([here, ahead, behind, jnp.roll(here, -1, 0), jnp.roll(here, 1, 0), jnp.roll(here, -1, 1), jnp.roll(here, 1, 1), jnp.roll(here, -1, 2), jnp.roll(here, 1, 2)], axis=0).astype(jnp.float32)
        real_half = near[..., :half]
        imag_half = near[..., half:]
        paired = jnp.stack([jnp.concatenate([real_half, -imag_half], axis=-1), jnp.concatenate([imag_half, real_half], axis=-1)], axis=-3)
        output = jnp.einsum('zyxbkj,bzyxcrj->zyxrck', blocks, paired)
        return output.reshape(here.shape)
    return lax.map(one_slice, jnp.arange(count_t, dtype=jnp.int32))

def least_squares(rows_re, rows_im, start_norm):
    count = len(rows_re[0])
    height_re = jnp.transpose(jnp.stack([jnp.stack(row) for row in rows_re]), (2, 0, 1))
    height_im = jnp.transpose(jnp.stack([jnp.stack(row) for row in rows_im]), (2, 0, 1))
    upper = jnp.concatenate([height_re, -height_im], axis=2)
    lower = jnp.concatenate([height_im, height_re], axis=2)
    stacked = jnp.concatenate([upper, lower], axis=1)
    normal = jnp.einsum('rik,rij->rkj', stacked, stacked, precision=lax.Precision.HIGHEST)
    target = start_norm[:, None] * stacked[:, 0, :]
    factor = jnp.linalg.cholesky(normal)
    middle = lax.linalg.triangular_solve(factor, target[:, :, None], left_side=True, lower=True)
    coefs = lax.linalg.triangular_solve(factor, middle, left_side=True, lower=True, transpose_a=True)[:, :, 0]
    return (coefs[:, :count], coefs[:, count:])

def reference(right_side, links):
    source = right_side.astype(jnp.float32)
    start_norm = jnp.sqrt(inner_pair(source, source)[0] + EPSILON)
    basis = [source / start_norm[:, None]]
    zero_row = jnp.zeros_like(start_norm)
    rows_re = [[zero_row for column in range(ITERS)] for height in range(ITERS + 1)]
    rows_im = [[zero_row for column in range(ITERS)] for height in range(ITERS + 1)]
    for column in range(ITERS):
        rounded = lax.optimization_barrier(apply_operator(basis[column].astype(jnp.bfloat16), links).astype(jnp.bfloat16))
        image = rounded.astype(jnp.float32)
        residue = image
        for earlier in range(column + 1):
            proj_re, proj_im = inner_pair(basis[earlier], image)
            rows_re[earlier][column] = proj_re
            rows_im[earlier][column] = proj_im
            residue = residue - combined(proj_re, proj_im, basis[earlier])
        length = jnp.sqrt(inner_pair(residue, residue)[0] + EPSILON)
        rows_re[column + 1][column] = length
        basis.append(residue / length[:, None])
    coef_re, coef_im = least_squares(rows_re, rows_im, start_norm)
    solution = jnp.zeros(source.shape, jnp.float32)
    for column in range(ITERS):
        solution = solution + combined(coef_re[:, column], coef_im[:, column], basis[column])
    return solution
```

```python
import jax
import jax.numpy as jnp
from jax import lax
from jax.sharding import PartitionSpec as P

ITERS = 3


EPSILON = 1e-06

AXES = ("ta", "gz", "xy")


def all_sum(value):
    for axis in AXES:
        size = lax.axis_size(axis)
        if size & (size - 1):
            value = lax.psum(value, axis)
            continue
        step = 1
        while step < size:
            value = value + lax.ppermute(value, axis, [(i, i ^ step) for i in range(size)])
            step *= 2
    return value


def neighbours(value):
    result = [value, None, None, None, None, None, None]
    for index, (axis, dim) in enumerate((("ta", 0), ("gz", 1), ("xy", 2))):
        size, length = (lax.axis_size(axis), value.shape[dim])
        up = [(i, (i + 1) % size) for i in range(size)]
        down = [(j, i) for i, j in up]
        last = lax.slice_in_dim(value, length - 1, length, axis=dim)
        first = lax.slice_in_dim(value, 0, 1, axis=dim)
        from_next = lax.ppermute(first, axis, down)
        from_prev = lax.ppermute(last, axis, up)
        ahead = jnp.concatenate([lax.slice_in_dim(value, 1, length, axis=dim), from_next], axis=dim)
        behind = jnp.concatenate([from_prev, lax.slice_in_dim(value, 0, length - 1, axis=dim)], axis=dim)
        result[1 + 2 * index] = ahead
        result[2 + 2 * index] = behind
    result.append(jnp.roll(value, -1, 3))
    result.append(jnp.roll(value, 1, 3))
    return result


def turned(field):
    half = field.shape[-1] // 2
    return jnp.concatenate([-field[..., half:], field[..., :half]], axis=-1)


def inner_pair(left, right):
    return (
        jnp.sum(left * right, axis=(0, 1, 2, 3, 5)),
        jnp.sum(turned(left) * right, axis=(0, 1, 2, 3, 5)),
    )


def combined(coef_re, coef_im, field):
    return coef_re[:, None] * field + coef_im[:, None] * turned(field)


def local_squares(field):
    return jnp.sum(field * field, axis=(0, 1, 2, 3, 5))


def hop_products(field, blocks, half):
    near = jnp.stack(neighbours(field), axis=0)
    real_half = near[..., :half]
    imag_half = near[..., half:]
    paired = jnp.stack(
        [
            jnp.concatenate([real_half, -imag_half], axis=-1),
            jnp.concatenate([imag_half, real_half], axis=-1),
        ],
        axis=-3,
    )
    paired = paired.reshape(9, blocks.shape[0], 2, field.shape[4], field.shape[5])
    output = jnp.einsum("sbkj,bscrj->srck", blocks, paired, preferred_element_type=jnp.float32)
    return output.reshape(field.shape).astype(jnp.bfloat16)


def least_squares(rows_re, rows_im, start_norm):
    count = len(rows_re[0])
    height = len(rows_re)
    stacked = []
    for i in range(height):
        stacked.append([rows_re[i][k] for k in range(count)] + [-rows_im[i][k] for k in range(count)])
    for i in range(height):
        stacked.append([rows_im[i][k] for k in range(count)] + [rows_re[i][k] for k in range(count)])
    size = 2 * count
    normal = [[None] * size for _ in range(size)]
    for k in range(size):
        for j in range(k + 1):
            total = stacked[0][k] * stacked[0][j]
            for i in range(1, 2 * height):
                total = total + stacked[i][k] * stacked[i][j]
            normal[k][j] = total
    target = [start_norm * stacked[0][k] for k in range(size)]
    factor = [[None] * size for _ in range(size)]
    for k in range(size):
        diag = normal[k][k]
        for m in range(k):
            diag = diag - factor[k][m] * factor[k][m]
        diag = jnp.sqrt(diag)
        factor[k][k] = diag
        for i in range(k + 1, size):
            entry = normal[i][k]
            for m in range(k):
                entry = entry - factor[i][m] * factor[k][m]
            factor[i][k] = entry / diag
    middle = [None] * size
    for i in range(size):
        entry = target[i]
        for m in range(i):
            entry = entry - factor[i][m] * middle[m]
        middle[i] = entry / factor[i][i]
    coefs = [None] * size
    for i in reversed(range(size)):
        entry = middle[i]
        for m in range(i + 1, size):
            entry = entry - factor[m][i] * coefs[m]
        coefs[i] = entry / factor[i][i]
    return (coefs[:count], coefs[count:])


def on_device(right_side, links):
    dims = right_side.shape
    half = dims[5] // 2
    sites = dims[0] * dims[1] * dims[2] * dims[3]
    blocks = links.reshape(sites, 9, half, dims[5])
    source = right_side.astype(jnp.float32)
    start_norm = jnp.sqrt(all_sum(local_squares(source)) + EPSILON)
    basis = [source / start_norm[:, None]]
    zero_row = jnp.zeros_like(start_norm)
    rows_re = [[zero_row for column in range(ITERS)] for height in range(ITERS + 1)]
    rows_im = [[zero_row for column in range(ITERS)] for height in range(ITERS + 1)]
    for column in range(ITERS):
        image = hop_products(basis[column].astype(jnp.bfloat16), blocks, half).astype(jnp.float32)
        parts = []
        for earlier in range(column + 1):
            parts.extend(inner_pair(basis[earlier], image))
        sums = all_sum(jnp.stack(parts))
        residue = image
        for earlier in range(column + 1):
            proj_re, proj_im = sums[2 * earlier], sums[2 * earlier + 1]
            rows_re[earlier][column] = proj_re
            rows_im[earlier][column] = proj_im
            residue = residue - combined(proj_re, proj_im, basis[earlier])
        length = jnp.sqrt(all_sum(local_squares(residue)) + EPSILON)
        rows_re[column + 1][column] = length
        if column + 1 < ITERS:
            basis.append(residue / length[:, None])
    coef_re, coef_im = least_squares(rows_re, rows_im, start_norm)
    solution = jnp.zeros(dims, jnp.float32)
    for column in range(ITERS):
        solution = solution + combined(coef_re[column], coef_im[column], basis[column])
    return solution


def solution(mesh):
    in_specs = (P("ta", "gz", "xy", None, None, None), P("ta", "gz", "xy", None, None, None, None))
    out_specs = P("ta", "gz", "xy", None, None, None)
    return jax.shard_map(
        on_device, mesh=mesh, in_specs=in_specs, out_specs=out_specs, check_vma=False
    )
```

```python
import jax
import jax.numpy as jnp
from jax import lax
from jax.sharding import PartitionSpec as P

ITERS = 3


EPSILON = 1e-06

AXES = ("ta", "gz", "xy")


def all_sum(value):
    for axis in AXES:
        size = lax.axis_size(axis)
        if size & (size - 1):
            value = lax.psum(value, axis)
            continue
        step = 1
        while step < size:
            value = value + lax.ppermute(value, axis, [(i, i ^ step) for i in range(size)])
            step *= 2
    return value


def neighbours(value):
    result = [value, None, None, None, None, None, None]
    for index, (axis, dim) in enumerate((("ta", 0), ("gz", 1), ("xy", 2))):
        size, length = (lax.axis_size(axis), value.shape[dim])
        up = [(i, (i + 1) % size) for i in range(size)]
        down = [(j, i) for i, j in up]
        last = lax.slice_in_dim(value, length - 1, length, axis=dim)
        first = lax.slice_in_dim(value, 0, 1, axis=dim)
        from_next = lax.ppermute(first, axis, down)
        from_prev = lax.ppermute(last, axis, up)
        ahead = jnp.concatenate([lax.slice_in_dim(value, 1, length, axis=dim), from_next], axis=dim)
        behind = jnp.concatenate([from_prev, lax.slice_in_dim(value, 0, length - 1, axis=dim)], axis=dim)
        result[1 + 2 * index] = ahead
        result[2 + 2 * index] = behind
    result.append(jnp.roll(value, -1, 3))
    result.append(jnp.roll(value, 1, 3))
    return result


def turned(field):
    half = field.shape[-1] // 2
    return jnp.concatenate([-field[..., half:], field[..., :half]], axis=-1)


def inner_pair(left, right):
    return (
        jnp.sum(left * right, axis=(0, 1, 2, 3, 5)),
        jnp.sum(turned(left) * right, axis=(0, 1, 2, 3, 5)),
    )


def combined(coef_re, coef_im, field):
    return coef_re[:, None] * field + coef_im[:, None] * turned(field)


def local_squares(field):
    return jnp.sum(field * field, axis=(0, 1, 2, 3, 5))


def hop_products(field, blocks, half):
    near = jnp.stack(neighbours(field), axis=0)
    real_half = near[..., :half]
    imag_half = near[..., half:]
    paired = jnp.stack(
        [
            jnp.concatenate([real_half, -imag_half], axis=-1),
            jnp.concatenate([imag_half, real_half], axis=-1),
        ],
        axis=-3,
    )
    paired = paired.reshape(9, blocks.shape[0], 2, field.shape[4], field.shape[5])
    output = jnp.einsum("sbkj,bscrj->srck", blocks, paired, preferred_element_type=jnp.float32)
    return output.reshape(field.shape).astype(jnp.bfloat16)


def least_squares(rows_re, rows_im, start_norm):
    count = len(rows_re[0])
    height = len(rows_re)
    stacked = []
    for i in range(height):
        stacked.append([rows_re[i][k] for k in range(count)] + [-rows_im[i][k] for k in range(count)])
    for i in range(height):
        stacked.append([rows_im[i][k] for k in range(count)] + [rows_re[i][k] for k in range(count)])
    size = 2 * count
    normal = [[None] * size for _ in range(size)]
    for k in range(size):
        for j in range(k + 1):
            total = stacked[0][k] * stacked[0][j]
            for i in range(1, 2 * height):
                total = total + stacked[i][k] * stacked[i][j]
            normal[k][j] = total
    target = [start_norm * stacked[0][k] for k in range(size)]
    factor = [[None] * size for _ in range(size)]
    for k in range(size):
        diag = normal[k][k]
        for m in range(k):
            diag = diag - factor[k][m] * factor[k][m]
        diag = jnp.sqrt(diag)
        factor[k][k] = diag
        for i in range(k + 1, size):
            entry = normal[i][k]
            for m in range(k):
                entry = entry - factor[i][m] * factor[k][m]
            factor[i][k] = entry / diag
    middle = [None] * size
    for i in range(size):
        entry = target[i]
        for m in range(i):
            entry = entry - factor[i][m] * middle[m]
        middle[i] = entry / factor[i][i]
    coefs = [None] * size
    for i in reversed(range(size)):
        entry = middle[i]
        for m in range(i + 1, size):
            entry = entry - factor[m][i] * coefs[m]
        coefs[i] = entry / factor[i][i]
    return (coefs[:count], coefs[count:])


def on_device(right_side, links):
    dims = right_side.shape
    half = dims[5] // 2
    sites = dims[0] * dims[1] * dims[2] * dims[3]
    blocks = links.reshape(sites, 9, half, dims[5])
    source = right_side.astype(jnp.float32)
    start_norm = jnp.sqrt(all_sum(local_squares(source)) + EPSILON)
    basis = [source / start_norm[:, None]]
    zero_row = jnp.zeros_like(start_norm)
    rows_re = [[zero_row for column in range(ITERS)] for height in range(ITERS + 1)]
    rows_im = [[zero_row for column in range(ITERS)] for height in range(ITERS + 1)]
    gram = {}
    for column in range(ITERS):
        image = hop_products(basis[column].astype(jnp.bfloat16), blocks, half).astype(jnp.float32)
        parts = [local_squares(image)]
        for earlier in range(column + 1):
            parts.extend(inner_pair(basis[earlier], image))
        for earlier in range(column + 1):
            parts.extend(inner_pair(basis[earlier], basis[column]))
        sums = all_sum(jnp.stack(parts))
        for earlier in range(column + 1):
            gram[earlier, column] = (sums[3 + 2 * (column + earlier)], sums[4 + 2 * (column + earlier)])
        residue = image
        for earlier in range(column + 1):
            proj_re, proj_im = sums[1 + 2 * earlier], sums[2 + 2 * earlier]
            rows_re[earlier][column] = proj_re
            rows_im[earlier][column] = proj_im
            residue = residue - combined(proj_re, proj_im, basis[earlier])
        squares = sums[0]
        for earlier in range(column + 1):
            size = rows_re[earlier][column] ** 2 + rows_im[earlier][column] ** 2
            squares = squares - 2.0 * size + gram[earlier, earlier][0] * size
        for first in range(column + 1):
            for second in range(first + 1, column + 1):
                a, b = rows_re[first][column], rows_im[first][column]
                c, d = rows_re[second][column], rows_im[second][column]
                g, q = gram[first, second]
                squares = squares + 2.0 * (g * (a * c + b * d) - q * (a * d - b * c))
        length = jnp.sqrt(jnp.maximum(squares, 0.0) + EPSILON)
        rows_re[column + 1][column] = length
        if column + 1 < ITERS:
            basis.append(residue / length[:, None])
    coef_re, coef_im = least_squares(rows_re, rows_im, start_norm)
    solution = jnp.zeros(dims, jnp.float32)
    for column in range(ITERS):
        solution = solution + combined(coef_re[column], coef_im[column], basis[column])
    return solution


def solution(mesh):
    in_specs = (P("ta", "gz", "xy", None, None, None), P("ta", "gz", "xy", None, None, None, None))
    out_specs = P("ta", "gz", "xy", None, None, None)
    return jax.shard_map(
        on_device, mesh=mesh, in_specs=in_specs, out_specs=out_specs, check_vma=False
    )
```

```python
import jax
import jax.numpy as jnp
from jax import lax
from jax.sharding import PartitionSpec as P

ITERS = 3


EPSILON = 1e-06

def exchanged(value, axis, mask):
    size = lax.axis_size(axis)
    return lax.ppermute(value, axis, [(i, i ^ mask) for i in range(size)])


def all_sum(value):
    for axis in ("gz", "ta", "xy"):
        size = lax.axis_size(axis)
        if size & (size - 1):
            value = lax.psum(value, axis)
            continue
        bits = size.bit_length() - 1
        lone = bits % 2
        if lone and axis == "gz":
            value = value + exchanged(value, axis, 1)
        mask = 1 << lone
        while mask < size:
            value = (value + exchanged(value, axis, mask)) + (
                exchanged(value, axis, 2 * mask) + exchanged(value, axis, 3 * mask)
            )
            mask *= 4
        if lone and axis != "gz":
            value = value + exchanged(value, axis, 1)
    return value


def neighbours(value):
    result = [value, None, None, None, None, None, None]
    for index, (axis, dim) in enumerate((("ta", 0), ("gz", 1), ("xy", 2))):
        size, length = (lax.axis_size(axis), value.shape[dim])
        up = [(i, (i + 1) % size) for i in range(size)]
        down = [(j, i) for i, j in up]
        last = lax.slice_in_dim(value, length - 1, length, axis=dim)
        first = lax.slice_in_dim(value, 0, 1, axis=dim)
        from_next = lax.ppermute(first, axis, down)
        from_prev = lax.ppermute(last, axis, up)
        ahead = jnp.concatenate([lax.slice_in_dim(value, 1, length, axis=dim), from_next], axis=dim)
        behind = jnp.concatenate([from_prev, lax.slice_in_dim(value, 0, length - 1, axis=dim)], axis=dim)
        result[1 + 2 * index] = ahead
        result[2 + 2 * index] = behind
    result.append(jnp.roll(value, -1, 3))
    result.append(jnp.roll(value, 1, 3))
    return result


def turned(field):
    half = field.shape[-1] // 2
    return jnp.concatenate([-field[..., half:], field[..., :half]], axis=-1)


def inner_pair(left, right):
    return (
        jnp.sum(left * right, axis=(0, 1, 2, 3, 5)),
        jnp.sum(turned(left) * right, axis=(0, 1, 2, 3, 5)),
    )


def combined(coef_re, coef_im, field):
    return coef_re[:, None] * field + coef_im[:, None] * turned(field)


def local_squares(field):
    return jnp.sum(field * field, axis=(0, 1, 2, 3, 5))


def hop_products(field, blocks, half):
    near = jnp.stack(neighbours(field), axis=0)
    real_half = near[..., :half]
    imag_half = near[..., half:]
    paired = jnp.stack(
        [
            jnp.concatenate([real_half, -imag_half], axis=-1),
            jnp.concatenate([imag_half, real_half], axis=-1),
        ],
        axis=-3,
    )
    paired = paired.reshape(9, blocks.shape[0], 2, field.shape[4], field.shape[5])
    output = jnp.einsum("sbkj,bscrj->srck", blocks, paired, preferred_element_type=jnp.float32)
    return output.reshape(field.shape).astype(jnp.bfloat16)


def least_squares(rows_re, rows_im, start_norm):
    count = len(rows_re[0])
    height = len(rows_re)
    stacked = []
    for i in range(height):
        stacked.append([rows_re[i][k] for k in range(count)] + [-rows_im[i][k] for k in range(count)])
    for i in range(height):
        stacked.append([rows_im[i][k] for k in range(count)] + [rows_re[i][k] for k in range(count)])
    size = 2 * count
    normal = [[None] * size for _ in range(size)]
    for k in range(size):
        for j in range(k + 1):
            total = stacked[0][k] * stacked[0][j]
            for i in range(1, 2 * height):
                total = total + stacked[i][k] * stacked[i][j]
            normal[k][j] = total
    target = [start_norm * stacked[0][k] for k in range(size)]
    factor = [[None] * size for _ in range(size)]
    for k in range(size):
        diag = normal[k][k]
        for m in range(k):
            diag = diag - factor[k][m] * factor[k][m]
        diag = jnp.sqrt(diag)
        factor[k][k] = diag
        for i in range(k + 1, size):
            entry = normal[i][k]
            for m in range(k):
                entry = entry - factor[i][m] * factor[k][m]
            factor[i][k] = entry / diag
    middle = [None] * size
    for i in range(size):
        entry = target[i]
        for m in range(i):
            entry = entry - factor[i][m] * middle[m]
        middle[i] = entry / factor[i][i]
    coefs = [None] * size
    for i in reversed(range(size)):
        entry = middle[i]
        for m in range(i + 1, size):
            entry = entry - factor[m][i] * coefs[m]
        coefs[i] = entry / factor[i][i]
    return (coefs[:count], coefs[count:])


def on_device(right_side, links):
    dims = right_side.shape
    half = dims[5] // 2
    sites = dims[0] * dims[1] * dims[2] * dims[3]
    blocks = links.reshape(sites, 9, half, dims[5])
    source = right_side.astype(jnp.float32)
    start_norm = jnp.sqrt(all_sum(local_squares(source)) + EPSILON)
    basis = [source / start_norm[:, None]]
    zero_row = jnp.zeros_like(start_norm)
    rows_re = [[zero_row for column in range(ITERS)] for height in range(ITERS + 1)]
    rows_im = [[zero_row for column in range(ITERS)] for height in range(ITERS + 1)]
    gram = {}
    for column in range(ITERS):
        image = hop_products(basis[column].astype(jnp.bfloat16), blocks, half).astype(jnp.float32)
        parts = [local_squares(image)]
        for earlier in range(column + 1):
            parts.extend(inner_pair(basis[earlier], image))
        for earlier in range(column + 1):
            parts.extend(inner_pair(basis[earlier], basis[column]))
        sums = all_sum(jnp.stack(parts))
        for earlier in range(column + 1):
            gram[earlier, column] = (sums[3 + 2 * (column + earlier)], sums[4 + 2 * (column + earlier)])
        residue = image
        for earlier in range(column + 1):
            proj_re, proj_im = sums[1 + 2 * earlier], sums[2 + 2 * earlier]
            rows_re[earlier][column] = proj_re
            rows_im[earlier][column] = proj_im
            residue = residue - combined(proj_re, proj_im, basis[earlier])
        squares = sums[0]
        for earlier in range(column + 1):
            size = rows_re[earlier][column] ** 2 + rows_im[earlier][column] ** 2
            squares = squares - 2.0 * size + gram[earlier, earlier][0] * size
        for first in range(column + 1):
            for second in range(first + 1, column + 1):
                a, b = rows_re[first][column], rows_im[first][column]
                c, d = rows_re[second][column], rows_im[second][column]
                g, q = gram[first, second]
                squares = squares + 2.0 * (g * (a * c + b * d) - q * (a * d - b * c))
        length = jnp.sqrt(jnp.maximum(squares, 0.0) + EPSILON)
        rows_re[column + 1][column] = length
        if column + 1 < ITERS:
            basis.append(residue / length[:, None])
    coef_re, coef_im = least_squares(rows_re, rows_im, start_norm)
    solution = jnp.zeros(dims, jnp.float32)
    for column in range(ITERS):
        solution = solution + combined(coef_re[column], coef_im[column], basis[column])
    return solution


def solution(mesh):
    in_specs = (P("ta", "gz", "xy", None, None, None), P("ta", "gz", "xy", None, None, None, None))
    out_specs = P("ta", "gz", "xy", None, None, None)
    return jax.shard_map(
        on_device, mesh=mesh, in_specs=in_specs, out_specs=out_specs, check_vma=False
    )
```

```python
import jax
import jax.numpy as jnp
from jax import lax
from jax.sharding import PartitionSpec as P

ITERS = 3


EPSILON = 1e-06

def exchanged(value, axis, mask):
    size = lax.axis_size(axis)
    return lax.ppermute(value, axis, [(i, i ^ mask) for i in range(size)])


def all_sum(value):
    for axis in ("gz", "ta", "xy"):
        size = lax.axis_size(axis)
        if size & (size - 1):
            value = lax.psum(value, axis)
            continue
        bits = size.bit_length() - 1
        lone = bits % 2
        if lone and axis == "gz":
            value = value + exchanged(value, axis, 1)
        mask = 1 << lone
        while mask < size:
            value = (value + exchanged(value, axis, mask)) + (
                exchanged(value, axis, 2 * mask) + exchanged(value, axis, 3 * mask)
            )
            mask *= 4
        if lone and axis != "gz":
            value = value + exchanged(value, axis, 1)
    return value


SPLIT = (("ta", 0), ("gz", 1), ("xy", 2))


def sent_faces(value):
    faces = []
    for axis, dim in SPLIT:
        size, length = (lax.axis_size(axis), value.shape[dim])
        up = [(i, (i + 1) % size) for i in range(size)]
        down = [(j, i) for i, j in up]
        first = lax.slice_in_dim(value, 0, 1, axis=dim)
        last = lax.slice_in_dim(value, length - 1, length, axis=dim)
        faces.append(lax.ppermute(first, axis, down))
        faces.append(lax.ppermute(last, axis, up))
    return faces


def neighbours(value, faces):
    result = [value]
    for index, (axis, dim) in enumerate(SPLIT):
        length = value.shape[dim]
        from_next, from_prev = faces[2 * index], faces[2 * index + 1]
        result.append(jnp.concatenate([lax.slice_in_dim(value, 1, length, axis=dim), from_next], axis=dim))
        result.append(jnp.concatenate([from_prev, lax.slice_in_dim(value, 0, length - 1, axis=dim)], axis=dim))
    result.append(jnp.roll(value, -1, 3))
    result.append(jnp.roll(value, 1, 3))
    return result


def turned(field):
    half = field.shape[-1] // 2
    return jnp.concatenate([-field[..., half:], field[..., :half]], axis=-1)


def inner_pair(left, right):
    return (
        jnp.sum(left * right, axis=(0, 1, 2, 3, 5)),
        jnp.sum(turned(left) * right, axis=(0, 1, 2, 3, 5)),
    )


def combined(coef_re, coef_im, field):
    return coef_re[:, None] * field + coef_im[:, None] * turned(field)


def local_squares(field):
    return jnp.sum(field * field, axis=(0, 1, 2, 3, 5))


def hop_products(field, faces, blocks, half):
    near = jnp.stack(neighbours(field, faces), axis=0)
    real_half = near[..., :half]
    imag_half = near[..., half:]
    paired = jnp.stack(
        [
            jnp.concatenate([real_half, -imag_half], axis=-1),
            jnp.concatenate([imag_half, real_half], axis=-1),
        ],
        axis=-3,
    )
    paired = paired.reshape(9, blocks.shape[0], 2, field.shape[4], field.shape[5])
    output = jnp.einsum("sbkj,bscrj->srck", blocks, paired, preferred_element_type=jnp.float32)
    return output.reshape(field.shape).astype(jnp.bfloat16)


def least_squares(rows_re, rows_im, start_norm):
    count = len(rows_re[0])
    height = len(rows_re)
    stacked = []
    for i in range(height):
        stacked.append([rows_re[i][k] for k in range(count)] + [-rows_im[i][k] for k in range(count)])
    for i in range(height):
        stacked.append([rows_im[i][k] for k in range(count)] + [rows_re[i][k] for k in range(count)])
    size = 2 * count
    normal = [[None] * size for _ in range(size)]
    for k in range(size):
        for j in range(k + 1):
            total = stacked[0][k] * stacked[0][j]
            for i in range(1, 2 * height):
                total = total + stacked[i][k] * stacked[i][j]
            normal[k][j] = total
    target = [start_norm * stacked[0][k] for k in range(size)]
    factor = [[None] * size for _ in range(size)]
    for k in range(size):
        diag = normal[k][k]
        for m in range(k):
            diag = diag - factor[k][m] * factor[k][m]
        diag = jnp.sqrt(diag)
        factor[k][k] = diag
        for i in range(k + 1, size):
            entry = normal[i][k]
            for m in range(k):
                entry = entry - factor[i][m] * factor[k][m]
            factor[i][k] = entry / diag
    middle = [None] * size
    for i in range(size):
        entry = target[i]
        for m in range(i):
            entry = entry - factor[i][m] * middle[m]
        middle[i] = entry / factor[i][i]
    coefs = [None] * size
    for i in reversed(range(size)):
        entry = middle[i]
        for m in range(i + 1, size):
            entry = entry - factor[m][i] * coefs[m]
        coefs[i] = entry / factor[i][i]
    return (coefs[:count], coefs[count:])


def on_device(right_side, links):
    dims = right_side.shape
    half = dims[5] // 2
    sites = dims[0] * dims[1] * dims[2] * dims[3]
    blocks = links.reshape(sites, 9, half, dims[5])
    source = right_side.astype(jnp.float32)
    source_faces = sent_faces(right_side)
    start_norm = jnp.sqrt(all_sum(local_squares(source)) + EPSILON)
    basis = [source / start_norm[:, None]]
    basis_faces = [[face.astype(jnp.float32) / start_norm[:, None] for face in source_faces]]
    zero_row = jnp.zeros_like(start_norm)
    rows_re = [[zero_row for column in range(ITERS)] for height in range(ITERS + 1)]
    rows_im = [[zero_row for column in range(ITERS)] for height in range(ITERS + 1)]
    gram = {}
    for column in range(ITERS):
        rounded = hop_products(
            basis[column].astype(jnp.bfloat16),
            [face.astype(jnp.bfloat16) for face in basis_faces[column]],
            blocks,
            half,
        )
        if column + 1 < ITERS:
            image_faces = sent_faces(rounded)
        image = rounded.astype(jnp.float32)
        parts = [local_squares(image)]
        for earlier in range(column + 1):
            parts.extend(inner_pair(basis[earlier], image))
        for earlier in range(column + 1):
            parts.extend(inner_pair(basis[earlier], basis[column]))
        sums = all_sum(jnp.stack(parts))
        for earlier in range(column + 1):
            gram[earlier, column] = (sums[3 + 2 * (column + earlier)], sums[4 + 2 * (column + earlier)])
        residue = image
        for earlier in range(column + 1):
            proj_re, proj_im = sums[1 + 2 * earlier], sums[2 + 2 * earlier]
            rows_re[earlier][column] = proj_re
            rows_im[earlier][column] = proj_im
            residue = residue - combined(proj_re, proj_im, basis[earlier])
        squares = sums[0]
        for earlier in range(column + 1):
            size = rows_re[earlier][column] ** 2 + rows_im[earlier][column] ** 2
            squares = squares - 2.0 * size + gram[earlier, earlier][0] * size
        for first in range(column + 1):
            for second in range(first + 1, column + 1):
                a, b = rows_re[first][column], rows_im[first][column]
                c, d = rows_re[second][column], rows_im[second][column]
                g, q = gram[first, second]
                squares = squares + 2.0 * (g * (a * c + b * d) - q * (a * d - b * c))
        length = jnp.sqrt(jnp.maximum(squares, 0.0) + EPSILON)
        rows_re[column + 1][column] = length
        if column + 1 < ITERS:
            basis.append(residue / length[:, None])
            faces = []
            for face in image_faces:
                face = face.astype(jnp.float32)
                for earlier in range(column + 1):
                    face = face - combined(
                        rows_re[earlier][column], rows_im[earlier][column], basis_faces[earlier][len(faces)]
                    )
                faces.append(face / length[:, None])
            basis_faces.append(faces)
    coef_re, coef_im = least_squares(rows_re, rows_im, start_norm)
    solution = jnp.zeros(dims, jnp.float32)
    for column in range(ITERS):
        solution = solution + combined(coef_re[column], coef_im[column], basis[column])
    return solution


def solution(mesh):
    in_specs = (P("ta", "gz", "xy", None, None, None), P("ta", "gz", "xy", None, None, None, None))
    out_specs = P("ta", "gz", "xy", None, None, None)
    return jax.shard_map(
        on_device, mesh=mesh, in_specs=in_specs, out_specs=out_specs, check_vma=False
    )
```

```python
import math

import jax
import jax.numpy as jnp
from jax import lax
from jax.sharding import PartitionSpec as P

ITERS = 3


EPSILON = 1e-06

ORDER = ("ta", "gz", "xy")


def exchanged(value, flips):
    masks = {}
    for axis, mask in flips:
        masks[axis] = masks.get(axis, 0) ^ mask
    names = tuple(axis for axis in ORDER if axis in masks)
    sizes = [lax.axis_size(axis) for axis in names]
    pairs = []
    for source in range(math.prod(sizes)):
        rest, target, scale = source, 0, 1
        for axis, size in reversed(list(zip(names, sizes))):
            target += ((rest % size) ^ masks[axis]) * scale
            rest //= size
            scale *= size
        pairs.append((source, target))
    return lax.ppermute(value, names if len(names) > 1 else names[0], pairs)


def all_sum(value):
    for axis in ORDER:
        size = lax.axis_size(axis)
        if size & (size - 1):
            value = lax.psum(value, axis)
    bits = {axis: [1 << k for k in range(lax.axis_size(axis).bit_length() - 1)] for axis in ORDER
            if not lax.axis_size(axis) & (lax.axis_size(axis) - 1)}
    order = []
    if bits.get("gz"):
        order.append(("gz", bits["gz"].pop(0)))
    for axis in ("ta", "gz", "xy"):
        order.extend((axis, mask) for mask in bits.get(axis, []))
    while len(order) >= 2:
        first, second = order.pop(0), order.pop(0)
        value = (value + exchanged(value, (first,))) + (
            exchanged(value, (second,)) + exchanged(value, (first, second))
        )
    if order:
        value = value + exchanged(value, (order[0],))
    return value


def neighbours(value):
    result = [value, None, None, None, None, None, None]
    for index, (axis, dim) in enumerate((("ta", 0), ("gz", 1), ("xy", 2))):
        size, length = (lax.axis_size(axis), value.shape[dim])
        up = [(i, (i + 1) % size) for i in range(size)]
        down = [(j, i) for i, j in up]
        last = lax.slice_in_dim(value, length - 1, length, axis=dim)
        first = lax.slice_in_dim(value, 0, 1, axis=dim)
        from_next = lax.ppermute(first, axis, down)
        from_prev = lax.ppermute(last, axis, up)
        ahead = jnp.concatenate([lax.slice_in_dim(value, 1, length, axis=dim), from_next], axis=dim)
        behind = jnp.concatenate([from_prev, lax.slice_in_dim(value, 0, length - 1, axis=dim)], axis=dim)
        result[1 + 2 * index] = ahead
        result[2 + 2 * index] = behind
    result.append(jnp.roll(value, -1, 3))
    result.append(jnp.roll(value, 1, 3))
    return result


def turned(field):
    half = field.shape[-1] // 2
    return jnp.concatenate([-field[..., half:], field[..., :half]], axis=-1)


def inner_pair(left, right):
    return (
        jnp.sum(left * right, axis=(0, 1, 2, 3, 5)),
        jnp.sum(turned(left) * right, axis=(0, 1, 2, 3, 5)),
    )


def combined(coef_re, coef_im, field):
    return coef_re[:, None] * field + coef_im[:, None] * turned(field)


def local_squares(field):
    return jnp.sum(field * field, axis=(0, 1, 2, 3, 5))


def hop_products(field, blocks, half):
    near = jnp.stack(neighbours(field), axis=0)
    real_half = near[..., :half]
    imag_half = near[..., half:]
    paired = jnp.stack(
        [
            jnp.concatenate([real_half, -imag_half], axis=-1),
            jnp.concatenate([imag_half, real_half], axis=-1),
        ],
        axis=-3,
    )
    paired = paired.reshape(9, blocks.shape[0], 2, field.shape[4], field.shape[5])
    output = jnp.einsum("sbkj,bscrj->srck", blocks, paired, preferred_element_type=jnp.float32)
    return output.reshape(field.shape).astype(jnp.bfloat16)


def least_squares(rows_re, rows_im, start_norm):
    count = len(rows_re[0])
    height = len(rows_re)
    stacked = []
    for i in range(height):
        stacked.append([rows_re[i][k] for k in range(count)] + [-rows_im[i][k] for k in range(count)])
    for i in range(height):
        stacked.append([rows_im[i][k] for k in range(count)] + [rows_re[i][k] for k in range(count)])
    size = 2 * count
    normal = [[None] * size for _ in range(size)]
    for k in range(size):
        for j in range(k + 1):
            total = stacked[0][k] * stacked[0][j]
            for i in range(1, 2 * height):
                total = total + stacked[i][k] * stacked[i][j]
            normal[k][j] = total
    target = [start_norm * stacked[0][k] for k in range(size)]
    factor = [[None] * size for _ in range(size)]
    for k in range(size):
        diag = normal[k][k]
        for m in range(k):
            diag = diag - factor[k][m] * factor[k][m]
        diag = jnp.sqrt(diag)
        factor[k][k] = diag
        for i in range(k + 1, size):
            entry = normal[i][k]
            for m in range(k):
                entry = entry - factor[i][m] * factor[k][m]
            factor[i][k] = entry / diag
    middle = [None] * size
    for i in range(size):
        entry = target[i]
        for m in range(i):
            entry = entry - factor[i][m] * middle[m]
        middle[i] = entry / factor[i][i]
    coefs = [None] * size
    for i in reversed(range(size)):
        entry = middle[i]
        for m in range(i + 1, size):
            entry = entry - factor[m][i] * coefs[m]
        coefs[i] = entry / factor[i][i]
    return (coefs[:count], coefs[count:])


def on_device(right_side, links):
    dims = right_side.shape
    half = dims[5] // 2
    sites = dims[0] * dims[1] * dims[2] * dims[3]
    blocks = links.reshape(sites, 9, half, dims[5])
    source = right_side.astype(jnp.float32)
    start_norm = jnp.sqrt(all_sum(local_squares(source)) + EPSILON)
    basis = [source / start_norm[:, None]]
    zero_row = jnp.zeros_like(start_norm)
    rows_re = [[zero_row for column in range(ITERS)] for height in range(ITERS + 1)]
    rows_im = [[zero_row for column in range(ITERS)] for height in range(ITERS + 1)]
    gram = {}
    for column in range(ITERS):
        image = hop_products(basis[column].astype(jnp.bfloat16), blocks, half).astype(jnp.float32)
        parts = [local_squares(image)]
        for earlier in range(column + 1):
            parts.extend(inner_pair(basis[earlier], image))
        for earlier in range(column + 1):
            parts.extend(inner_pair(basis[earlier], basis[column]))
        sums = all_sum(jnp.stack(parts))
        for earlier in range(column + 1):
            gram[earlier, column] = (sums[3 + 2 * (column + earlier)], sums[4 + 2 * (column + earlier)])
        residue = image
        for earlier in range(column + 1):
            proj_re, proj_im = sums[1 + 2 * earlier], sums[2 + 2 * earlier]
            rows_re[earlier][column] = proj_re
            rows_im[earlier][column] = proj_im
            residue = residue - combined(proj_re, proj_im, basis[earlier])
        squares = sums[0]
        for earlier in range(column + 1):
            size = rows_re[earlier][column] ** 2 + rows_im[earlier][column] ** 2
            squares = squares - 2.0 * size + gram[earlier, earlier][0] * size
        for first in range(column + 1):
            for second in range(first + 1, column + 1):
                a, b = rows_re[first][column], rows_im[first][column]
                c, d = rows_re[second][column], rows_im[second][column]
                g, q = gram[first, second]
                squares = squares + 2.0 * (g * (a * c + b * d) - q * (a * d - b * c))
        length = jnp.sqrt(jnp.maximum(squares, 0.0) + EPSILON)
        rows_re[column + 1][column] = length
        if column + 1 < ITERS:
            basis.append(residue / length[:, None])
    coef_re, coef_im = least_squares(rows_re, rows_im, start_norm)
    solution = jnp.zeros(dims, jnp.float32)
    for column in range(ITERS):
        solution = solution + combined(coef_re[column], coef_im[column], basis[column])
    return solution


def solution(mesh):
    in_specs = (P("ta", "gz", "xy", None, None, None), P("ta", "gz", "xy", None, None, None, None))
    out_specs = P("ta", "gz", "xy", None, None, None)
    return jax.shard_map(
        on_device, mesh=mesh, in_specs=in_specs, out_specs=out_specs, check_vma=False
    )
```

```python
import jax
import jax.numpy as jnp
from jax import lax
from jax.sharding import PartitionSpec as P

ITERS = 3


EPSILON = 1e-06

def exchanged(value, axis, mask):
    size = lax.axis_size(axis)
    return lax.ppermute(value, axis, [(i, i ^ mask) for i in range(size)])


def all_sum(value):
    for axis in ("gz", "ta", "xy"):
        size = lax.axis_size(axis)
        if size & (size - 1):
            value = lax.psum(value, axis)
            continue
        bits = size.bit_length() - 1
        lone = bits % 2
        if lone and axis == "gz":
            value = value + exchanged(value, axis, 1)
        mask = 1 << lone
        while mask < size:
            value = (value + exchanged(value, axis, mask)) + (
                exchanged(value, axis, 2 * mask) + exchanged(value, axis, 3 * mask)
            )
            mask *= 4
        if lone and axis != "gz":
            value = value + exchanged(value, axis, 1)
    return value


def neighbours(value):
    result = [value, None, None, None, None, None, None]
    for index, (axis, dim) in enumerate((("ta", 0), ("gz", 1), ("xy", 2))):
        size, length = (lax.axis_size(axis), value.shape[dim])
        up = [(i, (i + 1) % size) for i in range(size)]
        down = [(j, i) for i, j in up]
        last = lax.slice_in_dim(value, length - 1, length, axis=dim)
        first = lax.slice_in_dim(value, 0, 1, axis=dim)
        from_next = lax.ppermute(first, axis, down)
        from_prev = lax.ppermute(last, axis, up)
        ahead = jnp.concatenate([lax.slice_in_dim(value, 1, length, axis=dim), from_next], axis=dim)
        behind = jnp.concatenate([from_prev, lax.slice_in_dim(value, 0, length - 1, axis=dim)], axis=dim)
        result[1 + 2 * index] = ahead
        result[2 + 2 * index] = behind
    result.append(jnp.roll(value, -1, 3))
    result.append(jnp.roll(value, 1, 3))
    return result


def turned(field):
    half = field.shape[-1] // 2
    return jnp.concatenate([-field[..., half:], field[..., :half]], axis=-1)


def inner_pair(left, right):
    return (
        jnp.sum(left * right, axis=(0, 1, 2, 3, 5)),
        jnp.sum(turned(left) * right, axis=(0, 1, 2, 3, 5)),
    )


def combined(coef_re, coef_im, field):
    return coef_re[:, None] * field + coef_im[:, None] * turned(field)


def local_squares(field):
    return jnp.sum(field * field, axis=(0, 1, 2, 3, 5))


def hop_products(field, blocks, half):
    near = jnp.stack(neighbours(field), axis=0)
    real_half = near[..., :half]
    imag_half = near[..., half:]
    paired = jnp.stack(
        [
            jnp.concatenate([real_half, -imag_half], axis=-1),
            jnp.concatenate([imag_half, real_half], axis=-1),
        ],
        axis=-3,
    )
    paired = paired.reshape(9, blocks.shape[0], 2, field.shape[4], field.shape[5])
    output = jnp.einsum("sbkj,bscrj->srck", blocks, paired, preferred_element_type=jnp.float32)
    return output.reshape(field.shape).astype(jnp.bfloat16)


def least_squares(rows_re, rows_im, start_norm):
    count = len(rows_re[0])
    height = len(rows_re)
    stacked = []
    for i in range(height):
        stacked.append([rows_re[i][k] for k in range(count)] + [-rows_im[i][k] for k in range(count)])
    for i in range(height):
        stacked.append([rows_im[i][k] for k in range(count)] + [rows_re[i][k] for k in range(count)])
    size = 2 * count
    normal = [[None] * size for _ in range(size)]
    for k in range(size):
        for j in range(k + 1):
            total = stacked[0][k] * stacked[0][j]
            for i in range(1, 2 * height):
                total = total + stacked[i][k] * stacked[i][j]
            normal[k][j] = total
    target = [start_norm * stacked[0][k] for k in range(size)]
    factor = [[None] * size for _ in range(size)]
    for k in range(size):
        diag = normal[k][k]
        for m in range(k):
            diag = diag - factor[k][m] * factor[k][m]
        diag = jnp.sqrt(diag)
        factor[k][k] = diag
        for i in range(k + 1, size):
            entry = normal[i][k]
            for m in range(k):
                entry = entry - factor[i][m] * factor[k][m]
            factor[i][k] = entry / diag
    middle = [None] * size
    for i in range(size):
        entry = target[i]
        for m in range(i):
            entry = entry - factor[i][m] * middle[m]
        middle[i] = entry / factor[i][i]
    coefs = [None] * size
    for i in reversed(range(size)):
        entry = middle[i]
        for m in range(i + 1, size):
            entry = entry - factor[m][i] * coefs[m]
        coefs[i] = entry / factor[i][i]
    return (coefs[:count], coefs[count:])


def column_sums(image, basis):
    parts = [local_squares(image)]
    for vector in basis:
        parts.extend(inner_pair(vector, image))
    for vector in basis:
        parts.extend(inner_pair(vector, basis[-1]))
    return all_sum(jnp.stack(parts))


def on_device(right_side, links):
    dims = right_side.shape
    half = dims[5] // 2
    sites = dims[0] * dims[1] * dims[2] * dims[3]
    blocks = links.reshape(sites, 9, half, dims[5])
    source = right_side.astype(jnp.float32)
    first_image = hop_products(right_side, blocks, half).astype(jnp.float32)
    first_sums = all_sum(
        jnp.stack([local_squares(first_image), *inner_pair(source, first_image), local_squares(source)])
    )
    start_norm = jnp.sqrt(first_sums[3] + EPSILON)
    start_square = start_norm * start_norm
    basis = [source / start_norm[:, None]]
    zero_row = jnp.zeros_like(start_norm)
    rows_re = [[zero_row for column in range(ITERS)] for height in range(ITERS + 1)]
    rows_im = [[zero_row for column in range(ITERS)] for height in range(ITERS + 1)]
    gram = {}
    for column in range(ITERS):
        if column == 0:
            image = first_image / start_norm[:, None]
            sums = jnp.stack([*(first_sums[:4] / start_square), zero_row])
        else:
            image = hop_products(basis[column].astype(jnp.bfloat16), blocks, half).astype(jnp.float32)
            sums = column_sums(image, basis[: column + 1])
        for earlier in range(column + 1):
            gram[earlier, column] = (sums[3 + 2 * (column + earlier)], sums[4 + 2 * (column + earlier)])
        residue = image
        for earlier in range(column + 1):
            proj_re, proj_im = sums[1 + 2 * earlier], sums[2 + 2 * earlier]
            rows_re[earlier][column] = proj_re
            rows_im[earlier][column] = proj_im
            residue = residue - combined(proj_re, proj_im, basis[earlier])
        squares = sums[0]
        for earlier in range(column + 1):
            size = rows_re[earlier][column] ** 2 + rows_im[earlier][column] ** 2
            squares = squares - 2.0 * size + gram[earlier, earlier][0] * size
        for first in range(column + 1):
            for second in range(first + 1, column + 1):
                a, b = rows_re[first][column], rows_im[first][column]
                c, d = rows_re[second][column], rows_im[second][column]
                g, q = gram[first, second]
                squares = squares + 2.0 * (g * (a * c + b * d) - q * (a * d - b * c))
        length = jnp.sqrt(jnp.maximum(squares, 0.0) + EPSILON)
        rows_re[column + 1][column] = length
        if column + 1 < ITERS:
            basis.append(residue / length[:, None])
    coef_re, coef_im = least_squares(rows_re, rows_im, start_norm)
    solution = jnp.zeros(dims, jnp.float32)
    for column in range(ITERS):
        solution = solution + combined(coef_re[column], coef_im[column], basis[column])
    return solution


def solution(mesh):
    in_specs = (P("ta", "gz", "xy", None, None, None), P("ta", "gz", "xy", None, None, None, None))
    out_specs = P("ta", "gz", "xy", None, None, None)
    return jax.shard_map(
        on_device, mesh=mesh, in_specs=in_specs, out_specs=out_specs, check_vma=False
    )
```

```python
import jax
import jax.numpy as jnp
from jax import lax
from jax.sharding import PartitionSpec as P

ITERS = 3


EPSILON = 1e-06

def exchanged(value, axis, mask):
    size = lax.axis_size(axis)
    return lax.ppermute(value, axis, [(i, i ^ mask) for i in range(size)])


def all_sum(value):
    for axis in ("gz", "ta", "xy"):
        size = lax.axis_size(axis)
        if size & (size - 1):
            value = lax.psum(value, axis)
            continue
        bits = size.bit_length() - 1
        lone = bits % 2
        if lone and axis == "gz":
            value = value + exchanged(value, axis, 1)
        mask = 1 << lone
        while mask < size:
            value = (value + exchanged(value, axis, mask)) + (
                exchanged(value, axis, 2 * mask) + exchanged(value, axis, 3 * mask)
            )
            mask *= 4
        if lone and axis != "gz":
            value = value + exchanged(value, axis, 1)
    return value


def neighbours(value):
    result = [value, None, None, None, None, None, None]
    for index, (axis, dim) in enumerate((("ta", 0), ("gz", 1), ("xy", 2))):
        size, length = (lax.axis_size(axis), value.shape[dim])
        up = [(i, (i + 1) % size) for i in range(size)]
        down = [(j, i) for i, j in up]
        last = lax.slice_in_dim(value, length - 1, length, axis=dim)
        first = lax.slice_in_dim(value, 0, 1, axis=dim)
        from_next = lax.ppermute(first, axis, down)
        from_prev = lax.ppermute(last, axis, up)
        ahead = jnp.concatenate([lax.slice_in_dim(value, 1, length, axis=dim), from_next], axis=dim)
        behind = jnp.concatenate([from_prev, lax.slice_in_dim(value, 0, length - 1, axis=dim)], axis=dim)
        result[1 + 2 * index] = ahead
        result[2 + 2 * index] = behind
    result.append(jnp.roll(value, -1, 3))
    result.append(jnp.roll(value, 1, 3))
    return result


def turned(field):
    half = field.shape[-1] // 2
    return jnp.concatenate([-field[..., half:], field[..., :half]], axis=-1)


def inner_pair(left, right):
    return (
        jnp.sum(left * right, axis=(0, 1, 2, 3, 5)),
        jnp.sum(turned(left) * right, axis=(0, 1, 2, 3, 5)),
    )


def combined(coef_re, coef_im, field):
    return coef_re[:, None] * field + coef_im[:, None] * turned(field)


def local_squares(field):
    return jnp.sum(field * field, axis=(0, 1, 2, 3, 5))


def complex_blocks(links):
    half = links.shape[-1] // 2
    real, imag = links[..., :half], links[..., half:]
    return jnp.concatenate(
        [jnp.concatenate([real, -imag], axis=-1), jnp.concatenate([imag, real], axis=-1)], axis=-2
    )


def hop_products(field, blocks, half):
    near = jnp.stack(neighbours(field), axis=0)
    near = near.reshape(9, blocks.shape[0], field.shape[4], field.shape[5])
    output = jnp.einsum("sbkj,bsrj->srk", blocks, near, preferred_element_type=jnp.float32)
    return output.reshape(field.shape).astype(jnp.bfloat16)


def least_squares(rows_re, rows_im, start_norm):
    count = len(rows_re[0])
    height = len(rows_re)
    stacked = []
    for i in range(height):
        stacked.append([rows_re[i][k] for k in range(count)] + [-rows_im[i][k] for k in range(count)])
    for i in range(height):
        stacked.append([rows_im[i][k] for k in range(count)] + [rows_re[i][k] for k in range(count)])
    size = 2 * count
    normal = [[None] * size for _ in range(size)]
    for k in range(size):
        for j in range(k + 1):
            total = stacked[0][k] * stacked[0][j]
            for i in range(1, 2 * height):
                total = total + stacked[i][k] * stacked[i][j]
            normal[k][j] = total
    target = [start_norm * stacked[0][k] for k in range(size)]
    factor = [[None] * size for _ in range(size)]
    for k in range(size):
        diag = normal[k][k]
        for m in range(k):
            diag = diag - factor[k][m] * factor[k][m]
        diag = jnp.sqrt(diag)
        factor[k][k] = diag
        for i in range(k + 1, size):
            entry = normal[i][k]
            for m in range(k):
                entry = entry - factor[i][m] * factor[k][m]
            factor[i][k] = entry / diag
    middle = [None] * size
    for i in range(size):
        entry = target[i]
        for m in range(i):
            entry = entry - factor[i][m] * middle[m]
        middle[i] = entry / factor[i][i]
    coefs = [None] * size
    for i in reversed(range(size)):
        entry = middle[i]
        for m in range(i + 1, size):
            entry = entry - factor[m][i] * coefs[m]
        coefs[i] = entry / factor[i][i]
    return (coefs[:count], coefs[count:])


def column_sums(image, basis):
    parts = [local_squares(image)]
    for vector in basis:
        parts.extend(inner_pair(vector, image))
    for vector in basis:
        parts.extend(inner_pair(vector, basis[-1]))
    return all_sum(jnp.stack(parts))


def on_device(right_side, links):
    dims = right_side.shape
    half = dims[5] // 2
    sites = dims[0] * dims[1] * dims[2] * dims[3]
    blocks = complex_blocks(links).reshape(sites, 9, dims[5], dims[5])
    source = right_side.astype(jnp.float32)
    first_image = hop_products(right_side, blocks, half).astype(jnp.float32)
    first_sums = all_sum(
        jnp.stack([local_squares(first_image), *inner_pair(source, first_image), local_squares(source)])
    )
    start_norm = jnp.sqrt(first_sums[3] + EPSILON)
    start_square = start_norm * start_norm
    basis = [source / start_norm[:, None]]
    zero_row = jnp.zeros_like(start_norm)
    rows_re = [[zero_row for column in range(ITERS)] for height in range(ITERS + 1)]
    rows_im = [[zero_row for column in range(ITERS)] for height in range(ITERS + 1)]
    gram = {}
    for column in range(ITERS):
        if column == 0:
            image = first_image / start_norm[:, None]
            sums = jnp.stack([*(first_sums[:4] / start_square), zero_row])
        else:
            image = hop_products(basis[column].astype(jnp.bfloat16), blocks, half).astype(jnp.float32)
            sums = column_sums(image, basis[: column + 1])
        for earlier in range(column + 1):
            gram[earlier, column] = (sums[3 + 2 * (column + earlier)], sums[4 + 2 * (column + earlier)])
        residue = image
        for earlier in range(column + 1):
            proj_re, proj_im = sums[1 + 2 * earlier], sums[2 + 2 * earlier]
            rows_re[earlier][column] = proj_re
            rows_im[earlier][column] = proj_im
            residue = residue - combined(proj_re, proj_im, basis[earlier])
        squares = sums[0]
        for earlier in range(column + 1):
            size = rows_re[earlier][column] ** 2 + rows_im[earlier][column] ** 2
            squares = squares - 2.0 * size + gram[earlier, earlier][0] * size
        for first in range(column + 1):
            for second in range(first + 1, column + 1):
                a, b = rows_re[first][column], rows_im[first][column]
                c, d = rows_re[second][column], rows_im[second][column]
                g, q = gram[first, second]
                squares = squares + 2.0 * (g * (a * c + b * d) - q * (a * d - b * c))
        length = jnp.sqrt(jnp.maximum(squares, 0.0) + EPSILON)
        rows_re[column + 1][column] = length
        if column + 1 < ITERS:
            basis.append(residue / length[:, None])
    coef_re, coef_im = least_squares(rows_re, rows_im, start_norm)
    solution = jnp.zeros(dims, jnp.float32)
    for column in range(ITERS):
        solution = solution + combined(coef_re[column], coef_im[column], basis[column])
    return solution


def solution(mesh):
    in_specs = (P("ta", "gz", "xy", None, None, None), P("ta", "gz", "xy", None, None, None, None))
    out_specs = P("ta", "gz", "xy", None, None, None)
    return jax.shard_map(
        on_device, mesh=mesh, in_specs=in_specs, out_specs=out_specs, check_vma=False
    )
```

```python
import jax
import jax.numpy as jnp
from jax import lax
from jax.sharding import PartitionSpec as P

ITERS = 3


EPSILON = 1e-06

def exchanged(value, axis, mask):
    size = lax.axis_size(axis)
    return lax.ppermute(value, axis, [(i, i ^ mask) for i in range(size)])


def all_sum(value):
    for axis in ("gz", "ta", "xy"):
        size = lax.axis_size(axis)
        if size & (size - 1):
            value = lax.psum(value, axis)
            continue
        bits = size.bit_length() - 1
        lone = bits % 2
        if lone and axis == "gz":
            value = value + exchanged(value, axis, 1)
        mask = 1 << lone
        while mask < size:
            value = (value + exchanged(value, axis, mask)) + (
                exchanged(value, axis, 2 * mask) + exchanged(value, axis, 3 * mask)
            )
            mask *= 4
        if lone and axis != "gz":
            value = value + exchanged(value, axis, 1)
    return value


def neighbours(value):
    result = [value, None, None, None, None, None, None]
    for index, (axis, dim) in enumerate((("ta", 0), ("gz", 1), ("xy", 2))):
        size, length = (lax.axis_size(axis), value.shape[dim])
        up = [(i, (i + 1) % size) for i in range(size)]
        down = [(j, i) for i, j in up]
        last = lax.slice_in_dim(value, length - 1, length, axis=dim)
        first = lax.slice_in_dim(value, 0, 1, axis=dim)
        from_next = lax.ppermute(first, axis, down)
        from_prev = lax.ppermute(last, axis, up)
        ahead = jnp.concatenate([lax.slice_in_dim(value, 1, length, axis=dim), from_next], axis=dim)
        behind = jnp.concatenate([from_prev, lax.slice_in_dim(value, 0, length - 1, axis=dim)], axis=dim)
        result[1 + 2 * index] = ahead
        result[2 + 2 * index] = behind
    result.append(jnp.roll(value, -1, 3))
    result.append(jnp.roll(value, 1, 3))
    return result


def turned(field):
    half = field.shape[-1] // 2
    return jnp.concatenate([-field[..., half:], field[..., :half]], axis=-1)


def inner_pair(left, right):
    return (
        jnp.sum(left * right, axis=(0, 1, 2, 3, 5)),
        jnp.sum(turned(left) * right, axis=(0, 1, 2, 3, 5)),
    )


def combined(coef_re, coef_im, field):
    return coef_re[:, None] * field + coef_im[:, None] * turned(field)


def local_squares(field):
    return jnp.sum(field * field, axis=(0, 1, 2, 3, 5))


def complex_blocks(links):
    half = links.shape[-1] // 2
    real, imag = links[..., :half], links[..., half:]
    return jnp.concatenate(
        [jnp.concatenate([real, -imag], axis=-1), jnp.concatenate([imag, real], axis=-1)], axis=-2
    )


def hop_products(field, blocks, half):
    near = jnp.stack(neighbours(field), axis=0)
    near = near.reshape(9, blocks.shape[0], field.shape[4], field.shape[5])
    output = jnp.einsum("sbkj,bsrj->srk", blocks, near, preferred_element_type=jnp.float32)
    return output.reshape(field.shape)


def least_squares(rows_re, rows_im, start_norm):
    count = len(rows_re[0])
    height = len(rows_re)
    stacked = []
    for i in range(height):
        stacked.append([rows_re[i][k] for k in range(count)] + [-rows_im[i][k] for k in range(count)])
    for i in range(height):
        stacked.append([rows_im[i][k] for k in range(count)] + [rows_re[i][k] for k in range(count)])
    size = 2 * count
    normal = [[None] * size for _ in range(size)]
    for k in range(size):
        for j in range(k + 1):
            total = stacked[0][k] * stacked[0][j]
            for i in range(1, 2 * height):
                total = total + stacked[i][k] * stacked[i][j]
            normal[k][j] = total
    target = [start_norm * stacked[0][k] for k in range(size)]
    factor = [[None] * size for _ in range(size)]
    for k in range(size):
        diag = normal[k][k]
        for m in range(k):
            diag = diag - factor[k][m] * factor[k][m]
        diag = jnp.sqrt(diag)
        factor[k][k] = diag
        for i in range(k + 1, size):
            entry = normal[i][k]
            for m in range(k):
                entry = entry - factor[i][m] * factor[k][m]
            factor[i][k] = entry / diag
    middle = [None] * size
    for i in range(size):
        entry = target[i]
        for m in range(i):
            entry = entry - factor[i][m] * middle[m]
        middle[i] = entry / factor[i][i]
    coefs = [None] * size
    for i in reversed(range(size)):
        entry = middle[i]
        for m in range(i + 1, size):
            entry = entry - factor[m][i] * coefs[m]
        coefs[i] = entry / factor[i][i]
    return (coefs[:count], coefs[count:])


def column_sums(image, basis):
    parts = [local_squares(image)]
    for vector in basis:
        parts.extend(inner_pair(vector, image))
    for vector in basis:
        parts.extend(inner_pair(vector, basis[-1]))
    return all_sum(jnp.stack(parts))


def on_device(right_side, links):
    dims = right_side.shape
    half = dims[5] // 2
    sites = dims[0] * dims[1] * dims[2] * dims[3]
    blocks = complex_blocks(links).reshape(sites, 9, dims[5], dims[5])
    source = right_side.astype(jnp.float32)
    first_image = hop_products(right_side, blocks, half).astype(jnp.float32)
    first_sums = all_sum(
        jnp.stack([local_squares(first_image), *inner_pair(source, first_image), local_squares(source)])
    )
    start_norm = jnp.sqrt(first_sums[3] + EPSILON)
    start_square = start_norm * start_norm
    basis = [source / start_norm[:, None]]
    zero_row = jnp.zeros_like(start_norm)
    rows_re = [[zero_row for column in range(ITERS)] for height in range(ITERS + 1)]
    rows_im = [[zero_row for column in range(ITERS)] for height in range(ITERS + 1)]
    gram = {}
    for column in range(ITERS):
        if column == 0:
            image = first_image / start_norm[:, None]
            sums = jnp.stack([*(first_sums[:4] / start_square), zero_row])
        else:
            image = hop_products(basis[column].astype(jnp.bfloat16), blocks, half).astype(jnp.float32)
            sums = column_sums(image, basis[: column + 1])
        for earlier in range(column + 1):
            gram[earlier, column] = (sums[3 + 2 * (column + earlier)], sums[4 + 2 * (column + earlier)])
        residue = image
        for earlier in range(column + 1):
            proj_re, proj_im = sums[1 + 2 * earlier], sums[2 + 2 * earlier]
            rows_re[earlier][column] = proj_re
            rows_im[earlier][column] = proj_im
            residue = residue - combined(proj_re, proj_im, basis[earlier])
        squares = sums[0]
        for earlier in range(column + 1):
            size = rows_re[earlier][column] ** 2 + rows_im[earlier][column] ** 2
            squares = squares - 2.0 * size + gram[earlier, earlier][0] * size
        for first in range(column + 1):
            for second in range(first + 1, column + 1):
                a, b = rows_re[first][column], rows_im[first][column]
                c, d = rows_re[second][column], rows_im[second][column]
                g, q = gram[first, second]
                squares = squares + 2.0 * (g * (a * c + b * d) - q * (a * d - b * c))
        length = jnp.sqrt(jnp.maximum(squares, 0.0) + EPSILON)
        rows_re[column + 1][column] = length
        if column + 1 < ITERS:
            basis.append(residue / length[:, None])
    coef_re, coef_im = least_squares(rows_re, rows_im, start_norm)
    solution = jnp.zeros(dims, jnp.float32)
    for column in range(ITERS):
        solution = solution + combined(coef_re[column], coef_im[column], basis[column])
    return solution


def solution(mesh):
    in_specs = (P("ta", "gz", "xy", None, None, None), P("ta", "gz", "xy", None, None, None, None))
    out_specs = P("ta", "gz", "xy", None, None, None)
    return jax.shard_map(
        on_device, mesh=mesh, in_specs=in_specs, out_specs=out_specs, check_vma=False
    )
```

```python
import jax
import jax.numpy as jnp
from jax import lax
from jax.sharding import PartitionSpec as P

ITERS = 3


EPSILON = 1e-06

def exchanged(value, axis, mask):
    size = lax.axis_size(axis)
    return lax.ppermute(value, axis, [(i, i ^ mask) for i in range(size)])


def all_sum(value):
    for axis in ("gz", "ta", "xy"):
        size = lax.axis_size(axis)
        if size & (size - 1):
            value = lax.psum(value, axis)
            continue
        bits = size.bit_length() - 1
        lone = bits % 2
        if lone and axis == "gz":
            value = value + exchanged(value, axis, 1)
        mask = 1 << lone
        while mask < size:
            value = (value + exchanged(value, axis, mask)) + (
                exchanged(value, axis, 2 * mask) + exchanged(value, axis, 3 * mask)
            )
            mask *= 4
        if lone and axis != "gz":
            value = value + exchanged(value, axis, 1)
    return value


def neighbours(value):
    result = [value, None, None, None, None, None, None]
    for index, (axis, dim) in enumerate((("ta", 0), ("gz", 1), ("xy", 2))):
        size, length = (lax.axis_size(axis), value.shape[dim])
        up = [(i, (i + 1) % size) for i in range(size)]
        down = [(j, i) for i, j in up]
        last = lax.slice_in_dim(value, length - 1, length, axis=dim)
        first = lax.slice_in_dim(value, 0, 1, axis=dim)
        from_next = lax.ppermute(first, axis, down)
        from_prev = lax.ppermute(last, axis, up)
        ahead = jnp.concatenate([lax.slice_in_dim(value, 1, length, axis=dim), from_next], axis=dim)
        behind = jnp.concatenate([from_prev, lax.slice_in_dim(value, 0, length - 1, axis=dim)], axis=dim)
        result[1 + 2 * index] = ahead
        result[2 + 2 * index] = behind
    result.append(jnp.roll(value, -1, 3))
    result.append(jnp.roll(value, 1, 3))
    return result


def turned(field):
    half = field.shape[-1] // 2
    return jnp.concatenate([-field[..., half:], field[..., :half]], axis=-1)


def inner_pair(left, right):
    return (
        jnp.sum(left * right, axis=(0, 1, 2, 3, 5)),
        jnp.sum(turned(left) * right, axis=(0, 1, 2, 3, 5)),
    )


def combined(coef_re, coef_im, field):
    return coef_re[:, None] * field + coef_im[:, None] * turned(field)


def local_squares(field):
    return jnp.sum(field * field, axis=(0, 1, 2, 3, 5))


def complex_blocks(links):
    half = links.shape[-1] // 2
    real, imag = links[..., :half], links[..., half:]
    return jnp.concatenate(
        [jnp.concatenate([real, -imag], axis=-1), jnp.concatenate([imag, real], axis=-1)], axis=-2
    )


def hop_products(field, blocks, half):
    near = jnp.stack(neighbours(field), axis=-2)
    near = near.reshape(blocks.shape[0], field.shape[4], blocks.shape[2])
    output = jnp.einsum("srj,skj->srk", near, blocks, preferred_element_type=jnp.float32)
    return output.reshape(field.shape).astype(jnp.bfloat16)


def least_squares(rows_re, rows_im, start_norm):
    count = len(rows_re[0])
    height = len(rows_re)
    stacked = []
    for i in range(height):
        stacked.append([rows_re[i][k] for k in range(count)] + [-rows_im[i][k] for k in range(count)])
    for i in range(height):
        stacked.append([rows_im[i][k] for k in range(count)] + [rows_re[i][k] for k in range(count)])
    size = 2 * count
    normal = [[None] * size for _ in range(size)]
    for k in range(size):
        for j in range(k + 1):
            total = stacked[0][k] * stacked[0][j]
            for i in range(1, 2 * height):
                total = total + stacked[i][k] * stacked[i][j]
            normal[k][j] = total
    target = [start_norm * stacked[0][k] for k in range(size)]
    factor = [[None] * size for _ in range(size)]
    for k in range(size):
        diag = normal[k][k]
        for m in range(k):
            diag = diag - factor[k][m] * factor[k][m]
        diag = jnp.sqrt(diag)
        factor[k][k] = diag
        for i in range(k + 1, size):
            entry = normal[i][k]
            for m in range(k):
                entry = entry - factor[i][m] * factor[k][m]
            factor[i][k] = entry / diag
    middle = [None] * size
    for i in range(size):
        entry = target[i]
        for m in range(i):
            entry = entry - factor[i][m] * middle[m]
        middle[i] = entry / factor[i][i]
    coefs = [None] * size
    for i in reversed(range(size)):
        entry = middle[i]
        for m in range(i + 1, size):
            entry = entry - factor[m][i] * coefs[m]
        coefs[i] = entry / factor[i][i]
    return (coefs[:count], coefs[count:])


def column_sums(image, basis):
    parts = [local_squares(image)]
    for vector in basis:
        parts.extend(inner_pair(vector, image))
    for vector in basis:
        parts.extend(inner_pair(vector, basis[-1]))
    return all_sum(jnp.stack(parts))


def on_device(right_side, links):
    dims = right_side.shape
    half = dims[5] // 2
    sites = dims[0] * dims[1] * dims[2] * dims[3]
    blocks = jnp.swapaxes(complex_blocks(links).reshape(sites, 9, dims[5], dims[5]), 1, 2)
    blocks = blocks.reshape(sites, dims[5], 9 * dims[5])
    source = right_side.astype(jnp.float32)
    first_image = hop_products(right_side, blocks, half).astype(jnp.float32)
    first_sums = all_sum(
        jnp.stack([local_squares(first_image), *inner_pair(source, first_image), local_squares(source)])
    )
    start_norm = jnp.sqrt(first_sums[3] + EPSILON)
    start_square = start_norm * start_norm
    basis = [source / start_norm[:, None]]
    zero_row = jnp.zeros_like(start_norm)
    rows_re = [[zero_row for column in range(ITERS)] for height in range(ITERS + 1)]
    rows_im = [[zero_row for column in range(ITERS)] for height in range(ITERS + 1)]
    gram = {}
    for column in range(ITERS):
        if column == 0:
            image = first_image / start_norm[:, None]
            sums = jnp.stack([*(first_sums[:4] / start_square), zero_row])
        else:
            image = hop_products(basis[column].astype(jnp.bfloat16), blocks, half).astype(jnp.float32)
            sums = column_sums(image, basis[: column + 1])
        for earlier in range(column + 1):
            gram[earlier, column] = (sums[3 + 2 * (column + earlier)], sums[4 + 2 * (column + earlier)])
        residue = image
        for earlier in range(column + 1):
            proj_re, proj_im = sums[1 + 2 * earlier], sums[2 + 2 * earlier]
            rows_re[earlier][column] = proj_re
            rows_im[earlier][column] = proj_im
            residue = residue - combined(proj_re, proj_im, basis[earlier])
        squares = sums[0]
        for earlier in range(column + 1):
            size = rows_re[earlier][column] ** 2 + rows_im[earlier][column] ** 2
            squares = squares - 2.0 * size + gram[earlier, earlier][0] * size
        for first in range(column + 1):
            for second in range(first + 1, column + 1):
                a, b = rows_re[first][column], rows_im[first][column]
                c, d = rows_re[second][column], rows_im[second][column]
                g, q = gram[first, second]
                squares = squares + 2.0 * (g * (a * c + b * d) - q * (a * d - b * c))
        length = jnp.sqrt(jnp.maximum(squares, 0.0) + EPSILON)
        rows_re[column + 1][column] = length
        if column + 1 < ITERS:
            basis.append(residue / length[:, None])
    coef_re, coef_im = least_squares(rows_re, rows_im, start_norm)
    solution = jnp.zeros(dims, jnp.float32)
    for column in range(ITERS):
        solution = solution + combined(coef_re[column], coef_im[column], basis[column])
    return solution


def solution(mesh):
    in_specs = (P("ta", "gz", "xy", None, None, None), P("ta", "gz", "xy", None, None, None, None))
    out_specs = P("ta", "gz", "xy", None, None, None)
    return jax.shard_map(
        on_device, mesh=mesh, in_specs=in_specs, out_specs=out_specs, check_vma=False
    )
```
